32 devices in a mesh: slab: 8 (over z, y), coil: 4 (over x, core).
Axes of the slice: x: 2, y: 2, z: 4, core: 2. Of those that a mesh axis runs over, the one named last changes fastest.
Arguments:
- image: bfloat16 [2, 320, 256, 128], P(None, None, 'slab'), may hold values from -6 to 6
- coil_maps: bfloat16 [16, 320, 256, 128], P('coil', None, 'slab'), may hold values from -5 to 5
- y_data: bfloat16 [2, 16, 320, 128, 128], P(None, 'coil', 'slab'), may hold values from -6 to 6
- kz_lines: int32 [2, 320, 128], P(None, 'slab'), may hold values from -1 to 255, as said below
Outputs:
- gradient: bfloat16 [2, 320, 256, 128], P(None, 'coil', 'slab')
The draws below stay inside these ranges and needn't reach their ends.
Inputs may be any that keep to these rules, and one draw needn't show every extreme that they name: kz_lines[m, ky, :] lists distinct sampled kz of that ky row first and -1 in the unused slots after them; every row has at least one sampled kz; row 160 uses all 128 slots.
All inputs are finite; a program needn't handle non-finite values.
Results may differ from the reference program's by a relative error of at most 0.0061.
Values may be sent and summed in bfloat16 or wider, within the bound.
No kernel may reach another device: no remote copies, remote signals or barrier semaphores. Data moves between devices by JAX's collectives and lax.ppermute only.
A program may use at most 256 MiB of HBM per device.

```python
import math
import jax
import jax.numpy as jnp
from jax import lax

Y = 320
Z = 256
C = 16
M = 2
XR = 64
KCAP = 128


def draw_kz_lines(key, part):
    first_key, second_key = jax.random.split(jax.random.fold_in(key, 11))
    row_ids = jnp.arange(Y, dtype=jnp.int32)
    distance = jnp.abs(row_ids - Y // 2)
    low_count = max(KCAP // 8, 1)
    base_count = KCAP - (KCAP - low_count) * distance // (Y // 2)
    jitter = jax.random.randint(first_key, (M, Y), 0, low_count + 1)
    counts = jnp.clip(base_count[None, :] - jitter, 1, KCAP)
    counts = jnp.where(row_ids[None, :] == Y // 2, KCAP, counts)
    kz_ids = jnp.arange(Z, dtype=jnp.int32)
    kz_distance = jnp.abs(kz_ids - Z // 2)
    noise = jax.random.randint(second_key, (M, Y, Z), 0, 2 * Z)
    scores = (noise - kz_distance[None, None, :] + Z) * Z + kz_ids[None, None, :]
    unused, chosen = lax.top_k(scores, KCAP)
    slot_ids = jnp.arange(KCAP, dtype=jnp.int32)
    return jnp.where(slot_ids[None, None, :] < counts[:, :, None], chosen.astype(jnp.int32), -1).astype(jnp.int32)


def level_of(own_key, dims, pieces, low, largest):
    level, own = 1.0, jax.random.fold_in(own_key, 6)
    for position, blocks in pieces:
        draws = jnp.exp(jax.random.uniform(jax.random.fold_in(own, position), (blocks,), jnp.float32, low / len(pieces), largest / len(pieces)))
        level = level * jnp.repeat(draws, dims[position] // blocks).reshape([-1 if axis == position else 1 for axis in range(len(dims))])
    return level


def bell_draw(stream_key, extent, deviation, bound, cuts=(), kind=jnp.bfloat16):
    level = level_of(stream_key, extent, cuts, -0.22, 0.18) if cuts else 1.0
    entries = jax.random.normal(stream_key, extent, jnp.float32) * deviation * level
    return jnp.minimum(jnp.maximum(entries, -bound), bound).astype(kind)


def setup_inputs(seed: int = 0) -> dict:
    seeds = jax.random.split(jax.random.key(seed), 5)
    image = bell_draw(seeds[0], (M, Y, Z, 2 * XR), 1.0, 6.0, ((2, 8),))
    coil_maps = bell_draw(seeds[1], (C, Y, Z, 2 * XR), 0.35, 5.0, ((0, 4), (2, 8)))
    y_data = bell_draw(seeds[2], (M, C, Y, KCAP, 2 * XR), 1.0, 6.0, ((1, 4), (2, 8)))
    kz_lines = draw_kz_lines(jax.random.fold_in(seeds[4], 71), 0)
    return dict(image=image, coil_maps=coil_maps, y_data=y_data, kz_lines=kz_lines)


def dft_table(length):
    positions = jnp.arange(length, dtype=jnp.int32)
    phase = (positions[:, None] * positions[None, :] % length).astype(jnp.float32) * (2.0 * math.pi / length)
    factor = 1.0 / math.sqrt(length)
    cosine = jnp.cos(phase) * factor
    sine_part = jnp.sin(phase) * factor
    table = jnp.stack([jnp.stack([cosine, sine_part], -1), jnp.stack([-sine_part, cosine], -1)], 1)
    return table.astype(jnp.bfloat16)

def reference(image, coil_maps, y_data, kz_lines):
    y_table = dft_table(Y).astype(jnp.float32)
    z_table = dft_table(Z).astype(jnp.float32)
    y_adjoint = y_table.transpose(2, 3, 0, 1)
    z_adjoint = z_table.transpose(2, 3, 0, 1)
    row_ids = jnp.arange(Y, dtype=jnp.int32)[:, None]
    outputs = []
    for state_index in range(M):
        pixels = image[state_index].astype(jnp.float32).reshape(Y, Z, 2, XR)
        sampled = kz_lines[state_index] >= 0
        kz_index = jnp.maximum(kz_lines[state_index], 0).astype(jnp.int32)

        def per_coil(accumulated, inputs):
            sens_map, measured = inputs
            sens_map = sens_map.astype(jnp.float32).reshape(Y, Z, 2, XR)
            sens_real, sens_imag = (sens_map[:, :, 0], sens_map[:, :, 1])
            pix_real, pix_imag = (pixels[:, :, 0], pixels[:, :, 1])
            coil_image = jnp.stack([sens_real * pix_real - sens_imag * pix_imag, sens_real * pix_imag + sens_imag * pix_real], 2).astype(jnp.bfloat16)
            spectrum = jnp.einsum('koyp,yzpx->kzox', y_table, coil_image.astype(jnp.float32)).astype(jnp.bfloat16)
            kspace = jnp.einsum('joqp,kqpx->kjox', z_table, spectrum.astype(jnp.float32))
            picked = jnp.take_along_axis(kspace, kz_index[:, :, None, None], axis=1)
            measured = measured.astype(jnp.float32).reshape(Y, KCAP, 2, XR)
            residual = jnp.where(sampled[:, :, None, None], picked - measured, jnp.float32(0.0)).astype(jnp.bfloat16)
            kz_grid = jnp.zeros((Y, Z, 2, XR), jnp.float32).at[row_ids, kz_index].add(residual.astype(jnp.float32))
            adjoint_z = jnp.einsum('zoqp,kqpx->kzox', z_adjoint, kz_grid).astype(jnp.bfloat16)
            coil_back = jnp.einsum('yokp,kzpx->yzox', y_adjoint, adjoint_z.astype(jnp.float32))
            back_real, back_imag = (coil_back[:, :, 0], coil_back[:, :, 1])
            term = jnp.stack([sens_real * back_real + sens_imag * back_imag, sens_real * back_imag - sens_imag * back_real], 2)
            return (accumulated + term, None)
        start_total = jnp.zeros((Y, Z, 2, XR), jnp.float32)
        accumulated, unused = lax.scan(per_coil, start_total, (coil_maps, y_data[state_index]))
        outputs.append(accumulated.reshape(Y, Z, 2 * XR))
    return jnp.stack(outputs).astype(jnp.bfloat16)
```

```python
import math

import jax
import jax.numpy as jnp
from jax import lax
from jax.sharding import PartitionSpec as P

F32 = jnp.float32
BF16 = jnp.bfloat16


def cos_sin(length):
    positions = jnp.arange(length, dtype=jnp.int32)
    phase = (positions[:, None] * positions[None, :] % length).astype(F32) * (
        2.0 * math.pi / length
    )
    factor = 1.0 / math.sqrt(length)
    return (
        (jnp.cos(phase) * factor).astype(BF16),
        (jnp.sin(phase) * factor).astype(BF16),
    )


def turned(values):
    half = values.shape[-1] // 2
    return jnp.concatenate([-values[..., half:], values[..., :half]], axis=-1)


def dup_halves(values):
    half = values.shape[-1] // 2
    real = values[..., :half]
    imag = values[..., half:]
    return (
        jnp.concatenate([real, real], axis=-1),
        jnp.concatenate([imag, imag], axis=-1),
    )


def state_gradient(pixels, sens_real, sens_imag, measured, kz_lines, y_tab):
    y_count = pixels.shape[0]
    coil_image = (sens_real * pixels + sens_imag * turned(pixels)).astype(BF16)
    prod = jnp.einsum("ky,cyzl->ckzl", y_tab, coil_image, preferred_element_type=F32)
    spectrum = (prod[:, :y_count] - turned(prod[:, y_count:])).astype(BF16)
    gathered = lax.all_to_all(spectrum, "slab", split_axis=1, concat_axis=2, tiled=True)
    z_count = gathered.shape[2]
    z_cos, z_sin = cos_sin(z_count)
    z_tab = jnp.concatenate([z_cos, z_sin], axis=1)
    sampled = kz_lines >= 0
    kz_index = jnp.maximum(kz_lines, 0)
    onehot = (
        (kz_index[..., None] == jnp.arange(z_count, dtype=jnp.int32)) & sampled[..., None]
    ).astype(BF16)
    rows = jnp.einsum("kjq,qz->kjz", onehot, z_tab, preferred_element_type=F32).astype(BF16)
    rows_cos = rows[..., :z_count]
    rows_sin = rows[..., z_count:]
    k_cos = jnp.einsum("kjz,ckzl->ckjl", rows_cos, gathered, preferred_element_type=F32)
    k_sin = jnp.einsum("kjz,ckzl->ckjl", rows_sin, gathered, preferred_element_type=F32)
    kspace = k_cos - turned(k_sin)
    residual = jnp.where(
        sampled[None, :, :, None], kspace - measured.astype(F32), F32(0.0)
    ).astype(BF16)
    a_cos = jnp.einsum("kjz,ckjl->ckzl", rows_cos, residual, preferred_element_type=F32)
    a_sin = jnp.einsum("kjz,ckjl->ckzl", rows_sin, residual, preferred_element_type=F32)
    adjoint_z = (a_cos + turned(a_sin)).astype(BF16)
    returned = lax.all_to_all(adjoint_z, "slab", split_axis=2, concat_axis=1, tiled=True)
    prod_back = jnp.einsum("yk,ckzl->cyzl", y_tab, returned, preferred_element_type=F32)
    coil_back = prod_back[:, :y_count] + turned(prod_back[:, y_count:])
    term = sens_real * coil_back - sens_imag * turned(coil_back)
    partial = jnp.sum(term, axis=0)
    summed = lax.psum_scatter(partial, "coil", scatter_dimension=0, tiled=True)
    return summed.astype(BF16)


def shards(image, coil_maps, y_data, kz_lines):
    state_count, y_count = image.shape[0], image.shape[1]
    y_cos, y_sin = cos_sin(y_count)
    y_tab = jnp.concatenate([y_cos, y_sin], axis=0)
    sens_real, sens_imag = dup_halves(coil_maps.astype(F32))
    outputs = []
    for state in range(state_count):
        outputs.append(
            state_gradient(
                image[state].astype(F32),
                sens_real,
                sens_imag,
                y_data[state],
                kz_lines[state],
                y_tab,
            )
        )
    return jnp.stack(outputs)


def solution(mesh):
    in_specs = (
        P(None, None, "slab", None),
        P("coil", None, "slab", None),
        P(None, "coil", "slab", None, None),
        P(None, "slab", None),
    )
    out_specs = P(None, "coil", "slab", None)
    return jax.shard_map(shards, mesh=mesh, in_specs=in_specs, out_specs=out_specs, check_vma=False)
```

```python
import math

import jax
import jax.numpy as jnp
from jax import lax
from jax.sharding import PartitionSpec as P

F32 = jnp.float32
BF16 = jnp.bfloat16


def cos_sin(length):
    positions = jnp.arange(length, dtype=jnp.int32)
    phase = (positions[:, None] * positions[None, :] % length).astype(F32) * (
        2.0 * math.pi / length
    )
    factor = 1.0 / math.sqrt(length)
    return (
        (jnp.cos(phase) * factor).astype(BF16),
        (jnp.sin(phase) * factor).astype(BF16),
    )


def turned(values):
    half = values.shape[-1] // 2
    return jnp.concatenate([-values[..., half:], values[..., :half]], axis=-1)


def dup_halves(values):
    half = values.shape[-1] // 2
    real = values[..., :half]
    imag = values[..., half:]
    return (
        jnp.concatenate([real, real], axis=-1),
        jnp.concatenate([imag, imag], axis=-1),
    )


def with_turned(values, axis):
    return jnp.concatenate([values, turned(values)], axis=axis)


def chunk_gradient(pixels, sens_real, sens_imag, measured, kz_lines, y_fwd, y_back):
    y_count = pixels.shape[0]
    coil_image = (sens_real * pixels + sens_imag * turned(pixels)).astype(BF16)
    spectrum = jnp.einsum(
        "ky,cyzl->ckzl", y_fwd, with_turned(coil_image, 1), preferred_element_type=F32
    ).astype(BF16)
    gathered = lax.all_to_all(spectrum, "slab", split_axis=1, concat_axis=2, tiled=True)
    z_count = gathered.shape[2]
    z_cos, z_sin = cos_sin(z_count)
    sampled = kz_lines >= 0
    kz_index = jnp.maximum(kz_lines, 0)
    onehot = (
        (kz_index[..., None] == jnp.arange(z_count, dtype=jnp.int32)) & sampled[..., None]
    ).astype(BF16)
    z_fwd = jnp.concatenate([z_cos, -z_sin], axis=1)
    rows_fwd = jnp.einsum("kjq,qz->kjz", onehot, z_fwd, preferred_element_type=F32).astype(BF16)
    kspace = jnp.einsum(
        "kjz,ckzl->ckjl", rows_fwd, with_turned(gathered, 2), preferred_element_type=F32
    )
    residual = jnp.where(
        sampled[None, :, :, None], kspace - measured.astype(F32), F32(0.0)
    ).astype(BF16)
    rows_back = jnp.concatenate(
        [rows_fwd[..., :z_count], -rows_fwd[..., z_count:]], axis=1
    )
    adjoint_z = jnp.einsum(
        "kjz,ckjl->ckzl", rows_back, with_turned(residual, 2), preferred_element_type=F32
    ).astype(BF16)
    returned = lax.all_to_all(adjoint_z, "slab", split_axis=2, concat_axis=1, tiled=True)
    both = jnp.einsum(
        "yk,ckzl->cyzl", y_back, with_turned(returned, 1), preferred_element_type=F32
    )
    coil_back = both[:, :y_count]
    turned_back = both[:, y_count:]
    return jnp.sum(sens_real * coil_back - sens_imag * turned_back, axis=0)


def shards(image, coil_maps, y_data, kz_lines):
    state_count, y_count = image.shape[0], image.shape[1]
    coil_count = coil_maps.shape[0]
    group = 2 if coil_count % 2 == 0 else 1
    y_cos, y_sin = cos_sin(y_count)
    y_fwd = jnp.concatenate([y_cos, -y_sin], axis=1)
    y_back = jnp.concatenate(
        [jnp.concatenate([y_cos, y_sin], axis=1), jnp.concatenate([-y_sin, y_cos], axis=1)],
        axis=0,
    )
    sens_real, sens_imag = dup_halves(coil_maps.astype(F32))
    outputs = []
    for state in range(state_count):
        pixels = image[state].astype(F32)
        total = None
        for first in range(0, coil_count, group):
            part = chunk_gradient(
                pixels,
                sens_real[first : first + group],
                sens_imag[first : first + group],
                y_data[state, first : first + group],
                kz_lines[state],
                y_fwd,
                y_back,
            )
            total = part if total is None else total + part
        summed = lax.psum_scatter(total, "coil", scatter_dimension=0, tiled=True)
        outputs.append(summed.astype(BF16))
    return jnp.stack(outputs)


def solution(mesh):
    in_specs = (
        P(None, None, "slab", None),
        P("coil", None, "slab", None),
        P(None, "coil", "slab", None, None),
        P(None, "slab", None),
    )
    out_specs = P(None, "coil", "slab", None)
    return jax.shard_map(shards, mesh=mesh, in_specs=in_specs, out_specs=out_specs, check_vma=False)
```

```python
import math

import jax
import jax.numpy as jnp
from jax import lax
from jax.sharding import PartitionSpec as P

F32 = jnp.float32
BF16 = jnp.bfloat16


def cos_sin(length):
    positions = jnp.arange(length, dtype=jnp.int32)
    phase = (positions[:, None] * positions[None, :] % length).astype(F32) * (
        2.0 * math.pi / length
    )
    factor = 1.0 / math.sqrt(length)
    return (
        (jnp.cos(phase) * factor).astype(BF16),
        (jnp.sin(phase) * factor).astype(BF16),
    )


def turned(values):
    half = values.shape[-1] // 2
    return jnp.concatenate([-values[..., half:], values[..., :half]], axis=-1)


def dup_halves(values):
    half = values.shape[-1] // 2
    real = values[..., :half]
    imag = values[..., half:]
    return (
        jnp.concatenate([real, real], axis=-1),
        jnp.concatenate([imag, imag], axis=-1),
    )


def with_turned(values, axis):
    return jnp.concatenate([values, turned(values)], axis=axis)


def forward_y(pixels, sens_real, sens_imag, y_fwd):
    coil_image = (sens_real * pixels + sens_imag * turned(pixels)).astype(BF16)
    return jnp.einsum(
        "ky,cyzl->ckzl", y_fwd, with_turned(coil_image, 1), preferred_element_type=F32
    ).astype(BF16)


def middle_z(gathered, measured, kz_lines):
    z_count = gathered.shape[2]
    z_cos, z_sin = cos_sin(z_count)
    sampled = kz_lines >= 0
    kz_index = jnp.maximum(kz_lines, 0)
    onehot = (
        (kz_index[..., None] == jnp.arange(z_count, dtype=jnp.int32)) & sampled[..., None]
    ).astype(BF16)
    z_fwd = jnp.concatenate([z_cos, -z_sin], axis=1)
    rows_fwd = jnp.einsum("kjq,qz->kjz", onehot, z_fwd, preferred_element_type=F32).astype(BF16)
    kspace = jnp.einsum(
        "kjz,ckzl->ckjl", rows_fwd, with_turned(gathered, 2), preferred_element_type=F32
    )
    residual = jnp.where(
        sampled[None, :, :, None], kspace - measured.astype(F32), F32(0.0)
    ).astype(BF16)
    rows_back = jnp.concatenate([rows_fwd[..., :z_count], -rows_fwd[..., z_count:]], axis=1)
    return jnp.einsum(
        "kjz,ckjl->ckzl", rows_back, with_turned(residual, 2), preferred_element_type=F32
    ).astype(BF16)


def backward_y(returned, sens_real, sens_imag, y_back):
    y_count = returned.shape[1]
    both = jnp.einsum(
        "yk,ckzl->cyzl", y_back, with_turned(returned, 1), preferred_element_type=F32
    )
    coil_back = both[:, :y_count]
    turned_back = both[:, y_count:]
    return jnp.sum(sens_real * coil_back - sens_imag * turned_back, axis=0)


def to_ky_blocks(values):
    return lax.all_to_all(values, "slab", split_axis=1, concat_axis=2, tiled=True)


def to_z_slabs(values):
    return lax.all_to_all(values, "slab", split_axis=2, concat_axis=1, tiled=True)


def after(value, *others):
    if not others:
        return value
    return lax.optimization_barrier((value,) + tuple(others))[0]


def shards(image, coil_maps, y_data, kz_lines):
    state_count, y_count = image.shape[0], image.shape[1]
    coil_count = coil_maps.shape[0]
    group = 2 if coil_count % 2 == 0 else 1
    y_cos, y_sin = cos_sin(y_count)
    y_fwd = jnp.concatenate([y_cos, -y_sin], axis=1)
    y_back = jnp.concatenate(
        [jnp.concatenate([y_cos, y_sin], axis=1), jnp.concatenate([-y_sin, y_cos], axis=1)],
        axis=0,
    )
    sens_real, sens_imag = dup_halves(coil_maps.astype(F32))
    chunks = [(state, first) for state in range(state_count) for first in range(0, coil_count, group)]
    count = len(chunks)

    def sens_of(index):
        first = chunks[index][1]
        return sens_real[first : first + group], sens_imag[first : first + group]

    def forward(index):
        state = chunks[index][0]
        return forward_y(image[state].astype(F32), *sens_of(index), y_fwd)

    def middle(index, gathered):
        state, first = chunks[index]
        return middle_z(gathered, y_data[state, first : first + group], kz_lines[state])

    def backward(index, returned):
        return backward_y(returned, *sens_of(index), y_back)

    gathered = {0: to_ky_blocks(forward(0))}
    returned = {}
    partials = {}
    for step in range(1, count + 1):
        if step >= 2:
            partials[step - 2] = backward(step - 2, returned[step - 2])
        if step < count:
            spectrum = forward(step)
            if step >= 2:
                spectrum = after(spectrum, returned[step - 2])
            gathered[step] = to_ky_blocks(spectrum)
        adjoint_z = middle(step - 1, gathered[step - 1])
        holds = []
        if step < count:
            holds.append(gathered[step])
            if step >= 2:
                holds.append(partials[step - 2])
        elif step >= 2:
            holds.append(returned[step - 2])
        returned[step - 1] = to_z_slabs(after(adjoint_z, *holds))
    partials[count - 1] = backward(count - 1, returned[count - 1])
    outputs = []
    for state in range(state_count):
        total = None
        for index in range(count):
            if chunks[index][0] == state:
                total = partials[index] if total is None else total + partials[index]
        summed = lax.psum_scatter(total, "coil", scatter_dimension=0, tiled=True)
        outputs.append(summed.astype(BF16))
    return jnp.stack(outputs)


def solution(mesh):
    in_specs = (
        P(None, None, "slab", None),
        P("coil", None, "slab", None),
        P(None, "coil", "slab", None, None),
        P(None, "slab", None),
    )
    out_specs = P(None, "coil", "slab", None)
    return jax.shard_map(shards, mesh=mesh, in_specs=in_specs, out_specs=out_specs, check_vma=False)
```

```python
import math

import jax
import jax.numpy as jnp
from jax import lax
from jax.sharding import PartitionSpec as P

F32 = jnp.float32
BF16 = jnp.bfloat16


def cos_sin(length):
    positions = jnp.arange(length, dtype=jnp.int32)
    phase = (positions[:, None] * positions[None, :] % length).astype(F32) * (
        2.0 * math.pi / length
    )
    factor = 1.0 / math.sqrt(length)
    return (
        (jnp.cos(phase) * factor).astype(BF16),
        (jnp.sin(phase) * factor).astype(BF16),
    )


def turned(values):
    half = values.shape[-1] // 2
    return jnp.concatenate([-values[..., half:], values[..., :half]], axis=-1)


def dup_halves(values):
    half = values.shape[-1] // 2
    real = values[..., :half]
    imag = values[..., half:]
    return (
        jnp.concatenate([real, real], axis=-1),
        jnp.concatenate([imag, imag], axis=-1),
    )


def with_turned(values, axis):
    return jnp.concatenate([values, turned(values)], axis=axis)


def forward_y(pixels, sens_real, sens_imag, y_fwd):
    coil_image = (sens_real * pixels + sens_imag * turned(pixels)).astype(BF16)
    return jnp.einsum(
        "ky,cyzl->ckzl", y_fwd, with_turned(coil_image, 1), preferred_element_type=F32
    ).astype(BF16)


def middle_z(gathered, measured, kz_lines):
    z_count = gathered.shape[2]
    z_cos, z_sin = cos_sin(z_count)
    sampled = kz_lines >= 0
    kz_index = jnp.maximum(kz_lines, 0)
    onehot = (
        (kz_index[..., None] == jnp.arange(z_count, dtype=jnp.int32)) & sampled[..., None]
    ).astype(BF16)
    z_fwd = jnp.concatenate([z_cos, -z_sin], axis=1)
    rows_fwd = jnp.einsum("kjq,qz->kjz", onehot, z_fwd, preferred_element_type=F32).astype(BF16)
    kspace = jnp.einsum(
        "kjz,ckzl->ckjl", rows_fwd, with_turned(gathered, 2), preferred_element_type=F32
    )
    residual = jnp.where(
        sampled[None, :, :, None], kspace - measured.astype(F32), F32(0.0)
    ).astype(BF16)
    rows_back = jnp.concatenate([rows_fwd[..., :z_count], -rows_fwd[..., z_count:]], axis=1)
    return jnp.einsum(
        "kjz,ckjl->ckzl", rows_back, with_turned(residual, 2), preferred_element_type=F32
    ).astype(BF16)


def backward_y(returned, sens_real, sens_imag, y_back):
    y_count = returned.shape[1]
    both = jnp.einsum(
        "yk,ckzl->cyzl", y_back, with_turned(returned, 1), preferred_element_type=F32
    )
    coil_back = both[:, :y_count]
    turned_back = both[:, y_count:]
    return jnp.sum(sens_real * coil_back - sens_imag * turned_back, axis=0)


def to_ky_blocks(values):
    return lax.all_to_all(values, "slab", split_axis=1, concat_axis=2, tiled=True)


def to_z_slabs(values):
    return lax.all_to_all(values, "slab", split_axis=2, concat_axis=1, tiled=True)


def after(value, *others):
    if not others:
        return value
    return lax.optimization_barrier((value,) + tuple(others))[0]


def shards(image, coil_maps, y_data, kz_lines):
    state_count, y_count = image.shape[0], image.shape[1]
    coil_count = coil_maps.shape[0]
    group = 2 if coil_count % 2 == 0 else 1
    y_cos, y_sin = cos_sin(y_count)
    y_fwd = jnp.concatenate([y_cos, -y_sin], axis=1)
    y_back = jnp.concatenate(
        [jnp.concatenate([y_cos, y_sin], axis=1), jnp.concatenate([-y_sin, y_cos], axis=1)],
        axis=0,
    )
    sens_real, sens_imag = dup_halves(coil_maps)
    outputs = []
    previous = None
    for state in range(state_count):
        pixels = image[state].astype(F32)
        total = None
        for first in range(0, coil_count, group):
            chunk_real = sens_real[first : first + group].astype(F32)
            chunk_imag = sens_imag[first : first + group].astype(F32)
            spectrum = forward_y(pixels, chunk_real, chunk_imag, y_fwd)
            adjoint_z = middle_z(
                to_ky_blocks(spectrum), y_data[state, first : first + group], kz_lines[state]
            )
            if previous is not None and first + group >= coil_count:
                adjoint_z = after(adjoint_z, previous)
            part = backward_y(to_z_slabs(adjoint_z), chunk_real, chunk_imag, y_back)
            total = part if total is None else total + part
        summed = lax.psum_scatter(total, "coil", scatter_dimension=0, tiled=True)
        previous = summed
        outputs.append(summed.astype(BF16))
    return jnp.stack(outputs)


def solution(mesh):
    in_specs = (
        P(None, None, "slab", None),
        P("coil", None, "slab", None),
        P(None, "coil", "slab", None, None),
        P(None, "slab", None),
    )
    out_specs = P(None, "coil", "slab", None)
    return jax.shard_map(shards, mesh=mesh, in_specs=in_specs, out_specs=out_specs, check_vma=False)
```

```python
import math

import jax
import jax.numpy as jnp
from jax import lax
from jax.sharding import PartitionSpec as P

F32 = jnp.float32
BF16 = jnp.bfloat16


def cos_sin(length):
    positions = jnp.arange(length, dtype=jnp.int32)
    phase = (positions[:, None] * positions[None, :] % length).astype(F32) * (
        2.0 * math.pi / length
    )
    factor = 1.0 / math.sqrt(length)
    return (
        (jnp.cos(phase) * factor).astype(BF16),
        (jnp.sin(phase) * factor).astype(BF16),
    )


def turned(values):
    half = values.shape[-1] // 2
    return jnp.concatenate([-values[..., half:], values[..., :half]], axis=-1)


def dup_halves(values):
    half = values.shape[-1] // 2
    real = values[..., :half]
    imag = values[..., half:]
    return (
        jnp.concatenate([real, real], axis=-1),
        jnp.concatenate([imag, imag], axis=-1),
    )


def with_turned(values, axis):
    return jnp.concatenate([values, turned(values)], axis=axis)


def forward_y(pixels, sens_real, sens_imag, y_fwd):
    coil_image = (sens_real * pixels + sens_imag * turned(pixels)).astype(BF16)
    return jnp.einsum(
        "ky,cyzl->ckzl", y_fwd, with_turned(coil_image, 1), preferred_element_type=F32
    ).astype(BF16)


def middle_z(gathered, measured, kz_lines):
    z_count = gathered.shape[2]
    z_cos, z_sin = cos_sin(z_count)
    sampled = kz_lines >= 0
    kz_index = jnp.maximum(kz_lines, 0)
    onehot = (
        (kz_index[..., None] == jnp.arange(z_count, dtype=jnp.int32)) & sampled[..., None]
    ).astype(BF16)
    z_fwd = jnp.concatenate([z_cos, -z_sin], axis=1)
    rows_fwd = jnp.einsum("kjq,qz->kjz", onehot, z_fwd, preferred_element_type=F32).astype(BF16)
    kspace = jnp.einsum(
        "kjz,ckzl->ckjl", rows_fwd, with_turned(gathered, 2), preferred_element_type=F32
    )
    residual = jnp.where(
        sampled[None, :, :, None], kspace - measured.astype(F32), F32(0.0)
    ).astype(BF16)
    rows_back = jnp.concatenate([rows_fwd[..., :z_count], -rows_fwd[..., z_count:]], axis=1)
    return jnp.einsum(
        "kjz,ckjl->ckzl", rows_back, with_turned(residual, 2), preferred_element_type=F32
    ).astype(BF16)


def backward_y(returned, sens_real, sens_imag, y_back):
    y_count = returned.shape[1]
    both = jnp.einsum(
        "yk,ckzl->cyzl", y_back, with_turned(returned, 1), preferred_element_type=F32
    )
    coil_back = both[:, :y_count]
    turned_back = both[:, y_count:]
    return jnp.sum(sens_real * coil_back - sens_imag * turned_back, axis=0)


def to_ky_blocks(values):
    return lax.all_to_all(values, "slab", split_axis=1, concat_axis=2, tiled=True)


def to_z_slabs(values):
    return lax.all_to_all(values, "slab", split_axis=2, concat_axis=1, tiled=True)


def after(value, *others):
    if not others:
        return value
    return lax.optimization_barrier((value,) + tuple(others))[0]


def shards(image, coil_maps, y_data, kz_lines):
    state_count, y_count = image.shape[0], image.shape[1]
    coil_count = coil_maps.shape[0]
    group = 2 if coil_count % 2 == 0 else 1
    y_cos, y_sin = cos_sin(y_count)
    y_fwd = jnp.concatenate([y_cos, -y_sin], axis=1)
    y_back = jnp.concatenate(
        [jnp.concatenate([y_cos, y_sin], axis=1), jnp.concatenate([-y_sin, y_cos], axis=1)],
        axis=0,
    )
    sens_real, sens_imag = dup_halves(coil_maps)
    chunks = [(state, first) for state in range(state_count) for first in range(0, coil_count, group)]
    count = len(chunks)

    def sens_of(index):
        first = chunks[index][1]
        return (
            sens_real[first : first + group].astype(F32),
            sens_imag[first : first + group].astype(F32),
        )

    gathered = []
    for index, (state, first) in enumerate(chunks):
        spectrum = forward_y(image[state].astype(F32), *sens_of(index), y_fwd)
        if gathered:
            spectrum = after(spectrum, gathered[-1])
        gathered.append(to_ky_blocks(spectrum))
    adjoints = [
        middle_z(gathered[index], y_data[state, first : first + group], kz_lines[state])
        for index, (state, first) in enumerate(chunks)
    ]
    returned = []
    totals = {}
    outputs = {}
    for index, (state, first) in enumerate(chunks):
        holds = [returned[-1]] if returned else [gathered[-1]]
        if index + 1 < count:
            holds.append(adjoints[index + 1])
        else:
            holds.extend(totals[done] for done in outputs)
        returned.append(to_z_slabs(after(adjoints[index], *holds)))
        part = backward_y(returned[-1], *sens_of(index), y_back)
        totals[state] = part if state not in totals else totals[state] + part
        if first + group >= coil_count:
            outputs[state] = lax.psum_scatter(totals[state], "coil", scatter_dimension=0, tiled=True)
    return jnp.stack([outputs[state].astype(BF16) for state in range(state_count)])


def solution(mesh):
    in_specs = (
        P(None, None, "slab", None),
        P("coil", None, "slab", None),
        P(None, "coil", "slab", None, None),
        P(None, "slab", None),
    )
    out_specs = P(None, "coil", "slab", None)
    return jax.shard_map(shards, mesh=mesh, in_specs=in_specs, out_specs=out_specs, check_vma=False)
```

```python
import math

import jax
import jax.numpy as jnp
from jax import lax
from jax.sharding import PartitionSpec as P

F32 = jnp.float32
BF16 = jnp.bfloat16


def cos_sin(length):
    positions = jnp.arange(length, dtype=jnp.int32)
    phase = (positions[:, None] * positions[None, :] % length).astype(F32) * (
        2.0 * math.pi / length
    )
    factor = 1.0 / math.sqrt(length)
    return (
        (jnp.cos(phase) * factor).astype(BF16),
        (jnp.sin(phase) * factor).astype(BF16),
    )


def turned(values):
    half = values.shape[-1] // 2
    return jnp.concatenate([-values[..., half:], values[..., :half]], axis=-1)


def dup_halves(values):
    half = values.shape[-1] // 2
    real = values[..., :half]
    imag = values[..., half:]
    return (
        jnp.concatenate([real, real], axis=-1),
        jnp.concatenate([imag, imag], axis=-1),
    )


def with_turned(values, axis):
    return jnp.concatenate([values, turned(values)], axis=axis)


def forward_y(pixels, sens_real, sens_imag, y_fwd):
    coil_image = (sens_real * pixels + sens_imag * turned(pixels)).astype(BF16)
    return jnp.einsum(
        "ky,cyzl->ckzl", y_fwd, with_turned(coil_image, 1), preferred_element_type=F32
    ).astype(BF16)


def middle_z(gathered, measured, kz_lines):
    z_count = gathered.shape[2]
    z_cos, z_sin = cos_sin(z_count)
    sampled = kz_lines >= 0
    kz_index = jnp.maximum(kz_lines, 0)
    onehot = (
        (kz_index[..., None] == jnp.arange(z_count, dtype=jnp.int32)) & sampled[..., None]
    ).astype(BF16)
    z_fwd = jnp.concatenate([z_cos, -z_sin], axis=1)
    rows_fwd = jnp.einsum("kjq,qz->kjz", onehot, z_fwd, preferred_element_type=F32).astype(BF16)
    kspace = jnp.einsum(
        "kjz,ckzl->ckjl", rows_fwd, with_turned(gathered, 2), preferred_element_type=F32
    )
    residual = jnp.where(
        sampled[None, :, :, None], kspace - measured.astype(F32), F32(0.0)
    ).astype(BF16)
    rows_back = jnp.concatenate([rows_fwd[..., :z_count], -rows_fwd[..., z_count:]], axis=1)
    return jnp.einsum(
        "kjz,ckjl->ckzl", rows_back, with_turned(residual, 2), preferred_element_type=F32
    ).astype(BF16)


def backward_y(returned, sens_real, sens_imag, y_back):
    y_count = returned.shape[1]
    both = jnp.einsum(
        "yk,ckzl->cyzl", y_back, with_turned(returned, 1), preferred_element_type=F32
    )
    coil_back = both[:, :y_count]
    turned_back = both[:, y_count:]
    return jnp.sum(sens_real * coil_back - sens_imag * turned_back, axis=0)


def to_ky_blocks(values):
    return lax.all_to_all(values, "slab", split_axis=1, concat_axis=2, tiled=True)


def to_z_slabs(values):
    return lax.all_to_all(values, "slab", split_axis=2, concat_axis=1, tiled=True)


def after(value, *others):
    if not others:
        return value
    return lax.optimization_barrier((value,) + tuple(others))[0]


def shards(image, coil_maps, y_data, kz_lines):
    state_count, y_count = image.shape[0], image.shape[1]
    coil_count = coil_maps.shape[0]
    group = 2 if coil_count % 2 == 0 else 1
    y_cos, y_sin = cos_sin(y_count)
    y_fwd = jnp.concatenate([y_cos, -y_sin], axis=1)
    y_back = jnp.concatenate(
        [jnp.concatenate([y_cos, y_sin], axis=1), jnp.concatenate([-y_sin, y_cos], axis=1)],
        axis=0,
    )
    sens_real, sens_imag = dup_halves(coil_maps)
    outputs = []
    previous = None
    for state in range(state_count):
        pixels = image[state].astype(F32)
        total = None
        for first in range(0, coil_count, group):
            chunk_real = sens_real[first : first + group].astype(F32)
            chunk_imag = sens_imag[first : first + group].astype(F32)
            spectrum = forward_y(pixels, chunk_real, chunk_imag, y_fwd)
            adjoint_z = middle_z(
                to_ky_blocks(spectrum), y_data[state, first : first + group], kz_lines[state]
            )
            if previous is not None and first + group >= coil_count:
                adjoint_z = after(adjoint_z, previous)
            part = backward_y(to_z_slabs(adjoint_z), chunk_real, chunk_imag, y_back)
            total = part if total is None else total + part
        summed = lax.psum_scatter(total.astype(BF16), "coil", scatter_dimension=0, tiled=True)
        previous = summed
        outputs.append(summed)
    return jnp.stack(outputs)


def solution(mesh):
    in_specs = (
        P(None, None, "slab", None),
        P("coil", None, "slab", None),
        P(None, "coil", "slab", None, None),
        P(None, "slab", None),
    )
    out_specs = P(None, "coil", "slab", None)
    return jax.shard_map(shards, mesh=mesh, in_specs=in_specs, out_specs=out_specs, check_vma=False)
```

```python
import math

import jax
import jax.numpy as jnp
from jax import lax
from jax.sharding import PartitionSpec as P

F32 = jnp.float32
BF16 = jnp.bfloat16


def cos_sin(length):
    positions = jnp.arange(length, dtype=jnp.int32)
    phase = (positions[:, None] * positions[None, :] % length).astype(F32) * (
        2.0 * math.pi / length
    )
    factor = 1.0 / math.sqrt(length)
    return (
        (jnp.cos(phase) * factor).astype(BF16),
        (jnp.sin(phase) * factor).astype(BF16),
    )


def turned(values):
    half = values.shape[-1] // 2
    return jnp.concatenate([-values[..., half:], values[..., :half]], axis=-1)


def dup_halves(values):
    half = values.shape[-1] // 2
    real = values[..., :half]
    imag = values[..., half:]
    return (
        jnp.concatenate([real, real], axis=-1),
        jnp.concatenate([imag, imag], axis=-1),
    )


def with_turned(values, axis):
    return jnp.concatenate([values, turned(values)], axis=axis)


def forward_y(pixels, sens_real, sens_imag, y_fwd):
    coil_image = (sens_real * pixels + sens_imag * turned(pixels)).astype(BF16)
    return jnp.einsum(
        "ky,cyzl->ckzl", y_fwd, with_turned(coil_image, 1), preferred_element_type=F32
    ).astype(BF16)


def middle_z(gathered, measured, kz_lines):
    z_count = gathered.shape[2]
    z_cos, z_sin = cos_sin(z_count)
    sampled = kz_lines >= 0
    kz_index = jnp.maximum(kz_lines, 0)
    onehot = (
        (kz_index[..., None] == jnp.arange(z_count, dtype=jnp.int32)) & sampled[..., None]
    ).astype(BF16)
    z_fwd = jnp.concatenate([z_cos, -z_sin], axis=1)
    rows_fwd = jnp.einsum("kjq,qz->kjz", onehot, z_fwd, preferred_element_type=F32).astype(BF16)
    kspace = jnp.einsum(
        "kjz,ckzl->ckjl", rows_fwd, with_turned(gathered, 2), preferred_element_type=F32
    )
    residual = jnp.where(
        sampled[None, :, :, None], kspace - measured.astype(F32), F32(0.0)
    ).astype(BF16)
    rows_back = jnp.concatenate([rows_fwd[..., :z_count], -rows_fwd[..., z_count:]], axis=1)
    return jnp.einsum(
        "kjz,ckjl->ckzl", rows_back, with_turned(residual, 2), preferred_element_type=F32
    ).astype(BF16)


def backward_y(returned, sens_real, sens_imag, y_back):
    y_count = returned.shape[1]
    both = jnp.einsum(
        "yk,ckzl->cyzl", y_back, with_turned(returned, 1), preferred_element_type=F32
    )
    coil_back = both[:, :y_count]
    turned_back = both[:, y_count:]
    return jnp.sum(sens_real * coil_back - sens_imag * turned_back, axis=0)


def to_ky_blocks(values):
    return lax.all_to_all(values, "slab", split_axis=1, concat_axis=2, tiled=True)


def to_z_slabs(values):
    return lax.all_to_all(values, "slab", split_axis=2, concat_axis=1, tiled=True)


def after(value, *others):
    if not others:
        return value
    return lax.optimization_barrier((value,) + tuple(others))[0]


def shards(image, coil_maps, y_data, kz_lines):
    state_count, y_count = image.shape[0], image.shape[1]
    coil_count = coil_maps.shape[0]
    group = 2 if coil_count % 2 == 0 else 1
    y_cos, y_sin = cos_sin(y_count)
    y_fwd = jnp.concatenate([y_cos, -y_sin], axis=1)
    y_back = jnp.concatenate(
        [jnp.concatenate([y_cos, y_sin], axis=1), jnp.concatenate([-y_sin, y_cos], axis=1)],
        axis=0,
    )
    sens_real, sens_imag = dup_halves(coil_maps)
    outputs = []
    previous = None
    spectrum = None
    for state in range(state_count):
        total = None
        for first in range(0, coil_count, group):
            pixels = image[state]
            chunk_real = sens_real[first : first + group]
            chunk_imag = sens_imag[first : first + group]
            if spectrum is not None:
                pixels, chunk_real, chunk_imag, _ = lax.optimization_barrier(
                    (pixels, chunk_real, chunk_imag, spectrum)
                )
            pixels = pixels.astype(F32)
            chunk_real = chunk_real.astype(F32)
            chunk_imag = chunk_imag.astype(F32)
            spectrum = forward_y(pixels, chunk_real, chunk_imag, y_fwd)
            adjoint_z = middle_z(
                to_ky_blocks(spectrum), y_data[state, first : first + group], kz_lines[state]
            )
            if previous is not None and first + group >= coil_count:
                adjoint_z = after(adjoint_z, previous)
            part = backward_y(to_z_slabs(adjoint_z), chunk_real, chunk_imag, y_back)
            total = part if total is None else total + part
        summed = lax.psum_scatter(total.astype(BF16), "coil", scatter_dimension=0, tiled=True)
        previous = summed
        outputs.append(summed)
    return jnp.stack(outputs)


def solution(mesh):
    in_specs = (
        P(None, None, "slab", None),
        P("coil", None, "slab", None),
        P(None, "coil", "slab", None, None),
        P(None, "slab", None),
    )
    out_specs = P(None, "coil", "slab", None)
    return jax.shard_map(shards, mesh=mesh, in_specs=in_specs, out_specs=out_specs, check_vma=False)
```

```python
import math

import jax
import jax.numpy as jnp
from jax import lax
from jax.sharding import PartitionSpec as P

F32 = jnp.float32
BF16 = jnp.bfloat16


def cos_sin(length):
    positions = jnp.arange(length, dtype=jnp.int32)
    phase = (positions[:, None] * positions[None, :] % length).astype(F32) * (
        2.0 * math.pi / length
    )
    factor = 1.0 / math.sqrt(length)
    return (
        (jnp.cos(phase) * factor).astype(BF16),
        (jnp.sin(phase) * factor).astype(BF16),
    )


def turned(values):
    half = values.shape[-1] // 2
    return jnp.concatenate([-values[..., half:], values[..., :half]], axis=-1)


def dup_halves(values):
    half = values.shape[-1] // 2
    real = values[..., :half]
    imag = values[..., half:]
    return (
        jnp.concatenate([real, real], axis=-1),
        jnp.concatenate([imag, imag], axis=-1),
    )


def with_turned(values, axis):
    return jnp.concatenate([values, turned(values)], axis=axis)


def forward_y(pixels, sens_real, sens_imag, y_fwd):
    coil_image = (sens_real * pixels + sens_imag * turned(pixels)).astype(BF16)
    return jnp.einsum(
        "ky,cyzl->ckzl", y_fwd, with_turned(coil_image, 1), preferred_element_type=F32
    ).astype(BF16)


def middle_z(gathered, measured, kz_lines):
    z_count = gathered.shape[2]
    z_cos, z_sin = cos_sin(z_count)
    sampled = kz_lines >= 0
    kz_index = jnp.maximum(kz_lines, 0)
    onehot = (
        (kz_index[..., None] == jnp.arange(z_count, dtype=jnp.int32)) & sampled[..., None]
    ).astype(BF16)
    z_fwd = jnp.concatenate([z_cos, -z_sin], axis=1)
    rows_fwd = jnp.einsum("kjq,qz->kjz", onehot, z_fwd, preferred_element_type=F32).astype(BF16)
    kspace = jnp.einsum(
        "kjz,ckzl->ckjl", rows_fwd, with_turned(gathered, 2), preferred_element_type=F32
    )
    residual = jnp.where(
        sampled[None, :, :, None], kspace - measured.astype(F32), F32(0.0)
    ).astype(BF16)
    rows_back = jnp.concatenate([rows_fwd[..., :z_count], -rows_fwd[..., z_count:]], axis=1)
    return jnp.einsum(
        "kjz,ckjl->ckzl", rows_back, with_turned(residual, 2), preferred_element_type=F32
    ).astype(BF16)


def backward_y(returned, sens_real, sens_imag, y_back):
    y_count = returned.shape[1]
    both = jnp.einsum(
        "yk,ckzl->cyzl", y_back, with_turned(returned, 1), preferred_element_type=F32
    )
    coil_back = both[:, :y_count]
    turned_back = both[:, y_count:]
    return jnp.sum(sens_real * coil_back - sens_imag * turned_back, axis=0)


def to_ky_blocks(values):
    return lax.all_to_all(values, "slab", split_axis=1, concat_axis=2, tiled=True)


def to_z_slabs(values):
    return lax.all_to_all(values, "slab", split_axis=2, concat_axis=1, tiled=True)


def after(value, *others):
    if not others:
        return value
    return lax.optimization_barrier((value,) + tuple(others))[0]


def shards(image, coil_maps, y_data, kz_lines):
    state_count, y_count = image.shape[0], image.shape[1]
    coil_count = coil_maps.shape[0]
    group = 2 if coil_count % 2 == 0 else 1
    y_cos, y_sin = cos_sin(y_count)
    y_fwd = jnp.concatenate([y_cos, -y_sin], axis=1)
    y_back = jnp.concatenate(
        [jnp.concatenate([y_cos, y_sin], axis=1), jnp.concatenate([-y_sin, y_cos], axis=1)],
        axis=0,
    )
    sens_real, sens_imag = dup_halves(coil_maps)
    outputs = []
    previous = None
    spectrum = None
    first_gathered = None
    for state in range(state_count):
        total = None
        for first in range(0, coil_count, group):
            pixels = image[state]
            chunk_real = sens_real[first : first + group]
            chunk_imag = sens_imag[first : first + group]
            if spectrum is not None:
                pixels, chunk_real, chunk_imag, _ = lax.optimization_barrier(
                    (pixels, chunk_real, chunk_imag, spectrum)
                )
            pixels = pixels.astype(F32)
            chunk_real = chunk_real.astype(F32)
            chunk_imag = chunk_imag.astype(F32)
            spectrum = forward_y(pixels, chunk_real, chunk_imag, y_fwd)
            if first_gathered is not None and state == 0 and first == group:
                spectrum = after(spectrum, first_gathered)
            gathered = to_ky_blocks(spectrum)
            if first_gathered is None:
                first_gathered = gathered
            adjoint_z = middle_z(
                gathered, y_data[state, first : first + group], kz_lines[state]
            )
            if previous is not None and first + group >= coil_count:
                adjoint_z = after(adjoint_z, previous)
            part = backward_y(to_z_slabs(adjoint_z), chunk_real, chunk_imag, y_back)
            total = part if total is None else total + part
        summed = lax.psum_scatter(total.astype(BF16), "coil", scatter_dimension=0, tiled=True)
        previous = summed
        outputs.append(summed)
    return jnp.stack(outputs)


def solution(mesh):
    in_specs = (
        P(None, None, "slab", None),
        P("coil", None, "slab", None),
        P(None, "coil", "slab", None, None),
        P(None, "slab", None),
    )
    out_specs = P(None, "coil", "slab", None)
    return jax.shard_map(shards, mesh=mesh, in_specs=in_specs, out_specs=out_specs, check_vma=False)
```

```python
import math

import jax
import jax.numpy as jnp
from jax import lax
from jax.sharding import PartitionSpec as P

F32 = jnp.float32
BF16 = jnp.bfloat16


def cos_sin(length):
    positions = jnp.arange(length, dtype=jnp.int32)
    phase = (positions[:, None] * positions[None, :] % length).astype(F32) * (
        2.0 * math.pi / length
    )
    factor = 1.0 / math.sqrt(length)
    return (
        (jnp.cos(phase) * factor).astype(BF16),
        (jnp.sin(phase) * factor).astype(BF16),
    )


def turned(values):
    half = values.shape[-1] // 2
    return jnp.concatenate([-values[..., half:], values[..., :half]], axis=-1)


def dup_halves(values):
    half = values.shape[-1] // 2
    real = values[..., :half]
    imag = values[..., half:]
    return (
        jnp.concatenate([real, real], axis=-1),
        jnp.concatenate([imag, imag], axis=-1),
    )


def with_turned(values, axis):
    return jnp.concatenate([values, turned(values)], axis=axis)


def forward_y(pixels, sens_real, sens_imag, y_fwd):
    coil_image = (sens_real * pixels + sens_imag * turned(pixels)).astype(BF16)
    return jnp.einsum(
        "ky,cyzl->ckzl", y_fwd, with_turned(coil_image, 1), preferred_element_type=F32
    ).astype(BF16)


def middle_z(gathered, measured, kz_lines):
    z_count = gathered.shape[2]
    z_cos, z_sin = cos_sin(z_count)
    sampled = kz_lines >= 0
    kz_index = jnp.maximum(kz_lines, 0)
    onehot = (
        (kz_index[..., None] == jnp.arange(z_count, dtype=jnp.int32)) & sampled[..., None]
    ).astype(BF16)
    z_fwd = jnp.concatenate([z_cos, -z_sin], axis=1)
    rows_fwd = jnp.einsum("kjq,qz->kjz", onehot, z_fwd, preferred_element_type=F32).astype(BF16)
    kspace = jnp.einsum(
        "kjz,ckzl->ckjl", rows_fwd, with_turned(gathered, 2), preferred_element_type=F32
    )
    residual = jnp.where(
        sampled[None, :, :, None], kspace - measured.astype(F32), F32(0.0)
    ).astype(BF16)
    rows_back = jnp.concatenate([rows_fwd[..., :z_count], -rows_fwd[..., z_count:]], axis=1)
    return jnp.einsum(
        "kjz,ckjl->ckzl", rows_back, with_turned(residual, 2), preferred_element_type=F32
    ).astype(BF16)


def backward_y(returned, sens_real, sens_imag, y_back):
    y_count = returned.shape[1]
    both = jnp.einsum(
        "yk,ckzl->cyzl", y_back, with_turned(returned, 1), preferred_element_type=F32
    )
    coil_back = both[:, :y_count]
    turned_back = both[:, y_count:]
    return jnp.sum(sens_real * coil_back - sens_imag * turned_back, axis=0)


def to_ky_blocks(values):
    return lax.all_to_all(values, "slab", split_axis=1, concat_axis=2, tiled=True)


def to_z_slabs(values):
    return lax.all_to_all(values, "slab", split_axis=2, concat_axis=1, tiled=True)


def after(value, *others):
    if not others:
        return value
    return lax.optimization_barrier((value,) + tuple(others))[0]


def shards(image, coil_maps, y_data, kz_lines):
    state_count, y_count = image.shape[0], image.shape[1]
    coil_count = coil_maps.shape[0]
    group = 2 if coil_count % 2 == 0 else 1
    y_cos, y_sin = cos_sin(y_count)
    y_fwd = jnp.concatenate([y_cos, -y_sin], axis=1)
    y_back = jnp.concatenate(
        [jnp.concatenate([y_cos, y_sin], axis=1), jnp.concatenate([-y_sin, y_cos], axis=1)],
        axis=0,
    )
    outputs = []
    previous = None
    spectrum = None
    first_gathered = None
    for state in range(state_count):
        total = None
        for first in range(0, coil_count, group):
            pixels = image[state]
            chunk_real, chunk_imag = dup_halves(coil_maps[first : first + group])
            if spectrum is not None:
                pixels, chunk_real, chunk_imag, _ = lax.optimization_barrier(
                    (pixels, chunk_real, chunk_imag, spectrum)
                )
            pixels = pixels.astype(F32)
            chunk_real = chunk_real.astype(F32)
            chunk_imag = chunk_imag.astype(F32)
            spectrum = forward_y(pixels, chunk_real, chunk_imag, y_fwd)
            if first_gathered is not None and state == 0 and first == group:
                spectrum = after(spectrum, first_gathered)
            gathered = to_ky_blocks(spectrum)
            if first_gathered is None:
                first_gathered = gathered
            adjoint_z = middle_z(
                gathered, y_data[state, first : first + group], kz_lines[state]
            )
            if previous is not None and first + group >= coil_count:
                adjoint_z = after(adjoint_z, previous)
            part = backward_y(to_z_slabs(adjoint_z), chunk_real, chunk_imag, y_back)
            total = part if total is None else total + part
        summed = lax.psum_scatter(total.astype(BF16), "coil", scatter_dimension=0, tiled=True)
        previous = summed
        outputs.append(summed)
    return jnp.stack(outputs)


def solution(mesh):
    in_specs = (
        P(None, None, "slab", None),
        P("coil", None, "slab", None),
        P(None, "coil", "slab", None, None),
        P(None, "slab", None),
    )
    out_specs = P(None, "coil", "slab", None)
    return jax.shard_map(shards, mesh=mesh, in_specs=in_specs, out_specs=out_specs, check_vma=False)
```

```python
import math

import jax
import jax.numpy as jnp
from jax import lax
from jax.sharding import PartitionSpec as P

F32 = jnp.float32
BF16 = jnp.bfloat16


def cos_sin(length):
    positions = jnp.arange(length, dtype=jnp.int32)
    phase = (positions[:, None] * positions[None, :] % length).astype(F32) * (
        2.0 * math.pi / length
    )
    factor = 1.0 / math.sqrt(length)
    return (
        (jnp.cos(phase) * factor).astype(BF16),
        (jnp.sin(phase) * factor).astype(BF16),
    )


def turned(values):
    half = values.shape[-1] // 2
    return jnp.concatenate([-values[..., half:], values[..., :half]], axis=-1)


def dup_halves(values):
    half = values.shape[-1] // 2
    real = values[..., :half]
    imag = values[..., half:]
    return (
        jnp.concatenate([real, real], axis=-1),
        jnp.concatenate([imag, imag], axis=-1),
    )


def with_turned(values, axis):
    return jnp.concatenate([values, turned(values)], axis=axis)


def forward_y(pixels, sens_real, sens_imag, y_fwd):
    coil_image = (sens_real * pixels + sens_imag * turned(pixels)).astype(BF16)
    return jnp.einsum(
        "ky,cyzl->ckzl", y_fwd, with_turned(coil_image, 1), preferred_element_type=F32
    ).astype(BF16)


def middle_z(gathered, measured, kz_lines):
    z_count = gathered.shape[2]
    z_cos, z_sin = cos_sin(z_count)
    sampled = kz_lines >= 0
    kz_index = jnp.maximum(kz_lines, 0)
    onehot = (
        (kz_index[..., None] == jnp.arange(z_count, dtype=jnp.int32)) & sampled[..., None]
    ).astype(BF16)
    z_fwd = jnp.concatenate([z_cos, -z_sin], axis=1)
    rows_fwd = jnp.einsum("kjq,qz->kjz", onehot, z_fwd, preferred_element_type=F32).astype(BF16)
    kspace = jnp.einsum(
        "kjz,ckzl->ckjl", rows_fwd, with_turned(gathered, 2), preferred_element_type=F32
    )
    residual = jnp.where(
        sampled[None, :, :, None], kspace - measured.astype(F32), F32(0.0)
    ).astype(BF16)
    rows_back = jnp.concatenate([rows_fwd[..., :z_count], -rows_fwd[..., z_count:]], axis=1)
    return jnp.einsum(
        "kjz,ckjl->ckzl", rows_back, with_turned(residual, 2), preferred_element_type=F32
    ).astype(BF16)


def backward_y(returned, sens_real, sens_imag, y_back):
    y_count = returned.shape[1]
    both = jnp.einsum(
        "yk,ckzl->cyzl", y_back, with_turned(returned, 1), preferred_element_type=F32
    )
    coil_back = both[:, :y_count]
    turned_back = both[:, y_count:]
    return jnp.sum(sens_real * coil_back - sens_imag * turned_back, axis=0)


def to_ky_blocks(values):
    return lax.all_to_all(values, "slab", split_axis=1, concat_axis=2, tiled=True)


def to_z_slabs(values):
    return lax.all_to_all(values, "slab", split_axis=2, concat_axis=1, tiled=True)


def after(value, *others):
    if not others:
        return value
    return lax.optimization_barrier((value,) + tuple(others))[0]


def shards(image, coil_maps, y_data, kz_lines):
    state_count, y_count = image.shape[0], image.shape[1]
    coil_count = coil_maps.shape[0]
    group = 2 if coil_count % 2 == 0 else 1
    y_cos, y_sin = cos_sin(y_count)
    y_fwd = jnp.concatenate([y_cos, -y_sin], axis=1)
    y_back = jnp.concatenate(
        [jnp.concatenate([y_cos, y_sin], axis=1), jnp.concatenate([-y_sin, y_cos], axis=1)],
        axis=0,
    )
    outputs = []
    previous = None
    spectrum = None
    first_gathered = None
    for state in range(state_count):
        total = None
        for first in range(0, coil_count, group):
            pixels = image[state]
            chunk_real, chunk_imag = dup_halves(coil_maps[first : first + group])
            if spectrum is not None:
                pixels, chunk_real, chunk_imag, _ = lax.optimization_barrier(
                    (pixels, chunk_real, chunk_imag, spectrum)
                )
            pixels = pixels.astype(F32)
            chunk_real = chunk_real.astype(F32)
            chunk_imag = chunk_imag.astype(F32)
            spectrum = forward_y(pixels, chunk_real, chunk_imag, y_fwd)
            if first_gathered is not None and state == 0 and first == group:
                spectrum = after(spectrum, first_gathered)
            gathered = to_ky_blocks(spectrum)
            if first_gathered is None:
                first_gathered = gathered
            adjoint_z = middle_z(
                gathered, y_data[state, first : first + group], kz_lines[state]
            )
            if previous is not None and first + group >= coil_count:
                adjoint_z = after(adjoint_z, previous)
            returned = to_z_slabs(adjoint_z)
            z_local = returned.shape[2]
            if total is not None and state == state_count - 1 and first + group >= coil_count and z_local % 2 == 0:
                half = z_local // 2
                pieces = []
                sent = None
                for low in (0, half):
                    window = slice(low, low + half)
                    piece_in = returned[:, :, window]
                    if sent is not None:
                        piece_in = after(piece_in, sent)
                    part = backward_y(
                        piece_in, chunk_real[:, :, window], chunk_imag[:, :, window], y_back
                    )
                    sent = (total[:, window] + part).astype(BF16)
                    pieces.append(lax.psum_scatter(sent, "coil", scatter_dimension=0, tiled=True))
                summed = jnp.concatenate(pieces, axis=1)
                total = None
                break
            part = backward_y(returned, chunk_real, chunk_imag, y_back)
            total = part if total is None else total + part
        if total is not None:
            summed = lax.psum_scatter(total.astype(BF16), "coil", scatter_dimension=0, tiled=True)
        previous = summed
        outputs.append(summed)
    return jnp.stack(outputs)


def solution(mesh):
    in_specs = (
        P(None, None, "slab", None),
        P("coil", None, "slab", None),
        P(None, "coil", "slab", None, None),
        P(None, "slab", None),
    )
    out_specs = P(None, "coil", "slab", None)
    return jax.shard_map(shards, mesh=mesh, in_specs=in_specs, out_specs=out_specs, check_vma=False)
```

```python
import math

import jax
import jax.numpy as jnp
from jax import lax
from jax.sharding import PartitionSpec as P

F32 = jnp.float32
BF16 = jnp.bfloat16


def cos_sin(length):
    positions = jnp.arange(length, dtype=jnp.int32)
    phase = (positions[:, None] * positions[None, :] % length).astype(F32) * (
        2.0 * math.pi / length
    )
    factor = 1.0 / math.sqrt(length)
    return (
        (jnp.cos(phase) * factor).astype(BF16),
        (jnp.sin(phase) * factor).astype(BF16),
    )


def turned(values):
    half = values.shape[-1] // 2
    return jnp.concatenate([-values[..., half:], values[..., :half]], axis=-1)


def dup_halves(values):
    half = values.shape[-1] // 2
    real = values[..., :half]
    imag = values[..., half:]
    return (
        jnp.concatenate([real, real], axis=-1),
        jnp.concatenate([imag, imag], axis=-1),
    )


def with_turned(values, axis):
    return jnp.concatenate([values, turned(values)], axis=axis)


def forward_y(pixels, sens_real, sens_imag, y_fwd):
    coil_image = (sens_real * pixels + sens_imag * turned(pixels)).astype(BF16)
    return jnp.einsum(
        "ky,cyzl->ckzl", y_fwd, with_turned(coil_image, 1), preferred_element_type=F32
    ).astype(BF16)


def middle_z(gathered, measured, kz_lines):
    z_count = gathered.shape[2]
    z_cos, z_sin = cos_sin(z_count)
    sampled = kz_lines >= 0
    kz_index = jnp.maximum(kz_lines, 0)
    onehot = (
        (kz_index[..., None] == jnp.arange(z_count, dtype=jnp.int32)) & sampled[..., None]
    ).astype(BF16)
    z_fwd = jnp.concatenate([z_cos, -z_sin], axis=1)
    rows_fwd = jnp.einsum("kjq,qz->kjz", onehot, z_fwd, preferred_element_type=F32).astype(BF16)
    kspace = jnp.einsum(
        "kjz,ckzl->ckjl", rows_fwd, with_turned(gathered, 2), preferred_element_type=F32
    )
    residual = jnp.where(
        sampled[None, :, :, None], kspace - measured.astype(F32), F32(0.0)
    ).astype(BF16)
    rows_back = jnp.concatenate([rows_fwd[..., :z_count], -rows_fwd[..., z_count:]], axis=1)
    return jnp.einsum(
        "kjz,ckjl->ckzl", rows_back, with_turned(residual, 2), preferred_element_type=F32
    ).astype(BF16)


def backward_y(returned, sens_real, sens_imag, y_back):
    y_count = returned.shape[1]
    both = jnp.einsum(
        "yk,ckzl->cyzl", y_back, with_turned(returned, 1), preferred_element_type=F32
    )
    coil_back = both[:, :y_count]
    turned_back = both[:, y_count:]
    return jnp.sum(sens_real * coil_back - sens_imag * turned_back, axis=0)


def to_ky_blocks(values):
    return lax.all_to_all(values, "slab", split_axis=1, concat_axis=2, tiled=True)


def to_z_slabs(values):
    return lax.all_to_all(values, "slab", split_axis=2, concat_axis=1, tiled=True)


def after(value, *others):
    if not others:
        return value
    return lax.optimization_barrier((value,) + tuple(others))[0]


def shards(image, coil_maps, y_data, kz_lines):
    state_count, y_count = image.shape[0], image.shape[1]
    coil_count = coil_maps.shape[0]
    group = 1
    y_cos, y_sin = cos_sin(y_count)
    y_fwd = jnp.concatenate([y_cos, -y_sin], axis=1)
    y_back = jnp.concatenate(
        [jnp.concatenate([y_cos, y_sin], axis=1), jnp.concatenate([-y_sin, y_cos], axis=1)],
        axis=0,
    )
    outputs = []
    previous = None
    spectrum = None
    first_gathered = None
    for state in range(state_count):
        total = None
        for first in range(0, coil_count, group):
            pixels = image[state]
            chunk_real, chunk_imag = dup_halves(coil_maps[first : first + group])
            if spectrum is not None:
                pixels, chunk_real, chunk_imag, _ = lax.optimization_barrier(
                    (pixels, chunk_real, chunk_imag, spectrum)
                )
            pixels = pixels.astype(F32)
            chunk_real = chunk_real.astype(F32)
            chunk_imag = chunk_imag.astype(F32)
            spectrum = forward_y(pixels, chunk_real, chunk_imag, y_fwd)
            if first_gathered is not None and state == 0 and first == group:
                spectrum = after(spectrum, first_gathered)
            gathered = to_ky_blocks(spectrum)
            if first_gathered is None:
                first_gathered = gathered
            adjoint_z = middle_z(
                gathered, y_data[state, first : first + group], kz_lines[state]
            )
            if previous is not None and first + group >= coil_count:
                adjoint_z = after(adjoint_z, previous)
            part = backward_y(to_z_slabs(adjoint_z), chunk_real, chunk_imag, y_back)
            total = part if total is None else total + part
        summed = lax.psum_scatter(total.astype(BF16), "coil", scatter_dimension=0, tiled=True)
        previous = summed
        outputs.append(summed)
    return jnp.stack(outputs)


def solution(mesh):
    in_specs = (
        P(None, None, "slab", None),
        P("coil", None, "slab", None),
        P(None, "coil", "slab", None, None),
        P(None, "slab", None),
    )
    out_specs = P(None, "coil", "slab", None)
    return jax.shard_map(shards, mesh=mesh, in_specs=in_specs, out_specs=out_specs, check_vma=False)
```

```python
import math

import jax
import jax.numpy as jnp
from jax import lax
from jax.sharding import PartitionSpec as P

F32 = jnp.float32
BF16 = jnp.bfloat16


def cos_sin(length):
    positions = jnp.arange(length, dtype=jnp.int32)
    phase = (positions[:, None] * positions[None, :] % length).astype(F32) * (
        2.0 * math.pi / length
    )
    factor = 1.0 / math.sqrt(length)
    return (
        (jnp.cos(phase) * factor).astype(BF16),
        (jnp.sin(phase) * factor).astype(BF16),
    )


def turned(values):
    half = values.shape[-1] // 2
    return jnp.concatenate([-values[..., half:], values[..., :half]], axis=-1)


def dup_halves(values):
    half = values.shape[-1] // 2
    real = values[..., :half]
    imag = values[..., half:]
    return (
        jnp.concatenate([real, real], axis=-1),
        jnp.concatenate([imag, imag], axis=-1),
    )


def with_turned(values, axis):
    return jnp.concatenate([values, turned(values)], axis=axis)


def forward_y(pixels, sens_real, sens_imag, y_fwd):
    coil_image = (
        sens_real.astype(F32) * pixels.astype(F32)
        + sens_imag.astype(F32) * turned(pixels).astype(F32)
    ).astype(BF16)
    return jnp.einsum(
        "ky,cyzl->ckzl", y_fwd, with_turned(coil_image, 1), preferred_element_type=F32
    ).astype(BF16)


def middle_z(gathered, measured, kz_lines):
    z_count = gathered.shape[2]
    z_cos, z_sin = cos_sin(z_count)
    sampled = kz_lines >= 0
    kz_index = jnp.maximum(kz_lines, 0)
    onehot = (
        (kz_index[..., None] == jnp.arange(z_count, dtype=jnp.int32)) & sampled[..., None]
    ).astype(BF16)
    z_fwd = jnp.concatenate([z_cos, -z_sin], axis=1)
    rows_fwd = jnp.einsum("kjq,qz->kjz", onehot, z_fwd, preferred_element_type=F32).astype(BF16)
    kspace = jnp.einsum(
        "kjz,ckzl->ckjl", rows_fwd, with_turned(gathered, 2), preferred_element_type=F32
    )
    residual = jnp.where(
        sampled[None, :, :, None], kspace - measured.astype(F32), F32(0.0)
    ).astype(BF16)
    rows_back = jnp.concatenate([rows_fwd[..., :z_count], -rows_fwd[..., z_count:]], axis=1)
    return jnp.einsum(
        "kjz,ckjl->ckzl", rows_back, with_turned(residual, 2), preferred_element_type=F32
    ).astype(BF16)


def backward_y(returned, sens_real, sens_imag, y_back):
    y_count = returned.shape[1]
    both = jnp.einsum(
        "yk,ckzl->cyzl", y_back, with_turned(returned, 1), preferred_element_type=F32
    )
    coil_back = both[:, :y_count]
    turned_back = both[:, y_count:]
    return jnp.sum(sens_real * coil_back - sens_imag * turned_back, axis=0)


def to_ky_blocks(values):
    return lax.all_to_all(values, "slab", split_axis=1, concat_axis=2, tiled=True)


def to_z_slabs(values):
    return lax.all_to_all(values, "slab", split_axis=2, concat_axis=1, tiled=True)


def after(value, *others):
    if not others:
        return value
    return lax.optimization_barrier((value,) + tuple(others))[0]


def shards(image, coil_maps, y_data, kz_lines):
    state_count, y_count = image.shape[0], image.shape[1]
    coil_count = coil_maps.shape[0]
    group = 2 if coil_count % 2 == 0 else 1
    y_cos, y_sin = cos_sin(y_count)
    y_fwd = jnp.concatenate([y_cos, -y_sin], axis=1)
    y_back = jnp.concatenate(
        [jnp.concatenate([y_cos, y_sin], axis=1), jnp.concatenate([-y_sin, y_cos], axis=1)],
        axis=0,
    )
    outputs = []
    previous = None
    spectrum = None
    first_gathered = None
    for state in range(state_count):
        total = None
        for first in range(0, coil_count, group):
            pixels = image[state]
            chunk_real, chunk_imag = dup_halves(coil_maps[first : first + group])
            if spectrum is not None:
                pixels, chunk_real, chunk_imag, _ = lax.optimization_barrier(
                    (pixels, chunk_real, chunk_imag, spectrum)
                )
            spectrum = forward_y(pixels, chunk_real, chunk_imag, y_fwd)
            if first_gathered is not None and state == 0 and first == group:
                spectrum = after(spectrum, first_gathered)
            gathered = to_ky_blocks(spectrum)
            if first_gathered is None:
                first_gathered = gathered
            adjoint_z = middle_z(
                gathered, y_data[state, first : first + group], kz_lines[state]
            )
            if previous is not None and first + group >= coil_count:
                adjoint_z = after(adjoint_z, previous)
            part = backward_y(to_z_slabs(adjoint_z), chunk_real, chunk_imag, y_back)
            total = part if total is None else total + part
        summed = lax.psum_scatter(total.astype(BF16), "coil", scatter_dimension=0, tiled=True)
        previous = summed
        outputs.append(summed)
    return jnp.stack(outputs)


def solution(mesh):
    in_specs = (
        P(None, None, "slab", None),
        P("coil", None, "slab", None),
        P(None, "coil", "slab", None, None),
        P(None, "slab", None),
    )
    out_specs = P(None, "coil", "slab", None)
    return jax.shard_map(shards, mesh=mesh, in_specs=in_specs, out_specs=out_specs, check_vma=False)
```
